512 devices in a mesh: dp: 32 (over z, core), freq: 16 (over x, y).
Axes of the slice: x: 4, y: 4, z: 16, core: 2. Of those that a mesh axis runs over, the one named last changes fastest.
Arguments:
- output_grad: bfloat16 [1024, 384, 1024], P(('dp', 'freq')), may hold values from -6 to 6
- layer_input: bfloat16 [1024, 384, 1024], P(('dp', 'freq')), may hold values from -6 to 6
- counts: int32 [512], P(('dp', 'freq')), may hold values from 0 to 2, as said below
- bin_order: int32 [64], replicated, may hold values from 0 to 1023, as said below
- inverse_factor: bfloat16 [64, 2, 384, 384], P('freq'), may hold values from -0.10306207 to 0.70406207
Outputs:
- input_spectra_grad: bfloat16 [1024, 128, 384], P(('dp', 'freq'))
- tap_grad: float32 [9, 384, 384], P(None, 'dp', 'freq')
The draws below stay inside these ranges and needn't reach their ends.
Inputs may be any that keep to these rules, and one draw needn't show every extreme that they name: `counts`: slots at or past a shard's count hold no image; some shard has all 2 slots live and some has none. `bin_order`: entries are distinct bins of the 32 x 32 grid; slot j belongs to freq index j // 4.
All inputs are finite; a program needn't handle non-finite values.
Results may differ from the reference program's by a relative error of at most 0.0071.
Values may be sent and summed in bfloat16 or wider, within the bound.
No kernel may reach another device: no remote copies, remote signals or barrier semaphores. Data moves between devices by JAX's collectives and lax.ppermute only.
A program may use at most 64 MiB of HBM per device.

```python
import math
import jax
import jax.numpy as jnp
from jax import lax

C = 384
GRID = 32
TAPS = 9
SLOTS = 2
PIX = 1024
SHARDS = 512
IMAGES = 1024
BINS = 64


def draw_counts(key, part):
    first_key, second_key = jax.random.split(key)
    levels = jax.random.randint(first_key, (SHARDS,), 0, 6)
    values = jnp.where(levels >= 5, SLOTS, jnp.where(levels >= 3, (SLOTS + 1) // 2, 0))
    position = jax.random.randint(second_key, (), 0, SHARDS)
    values = values.at[position].set(SLOTS)
    values = values.at[(position + 1) % SHARDS].set(0)
    return values.astype(jnp.int32)


def draw_bin_order(key, part):
    first_key, second_key = jax.random.split(key)
    middle = jax.random.permutation(first_key, GRID * GRID - 2)[:BINS - 2] + 1
    ends = jnp.array([0, GRID * GRID - 1], dtype=jnp.int32)
    chosen = jnp.concatenate([middle.astype(jnp.int32), ends])
    return jax.random.permutation(second_key, chosen).astype(jnp.int32)


def draw_inverse_factor(key, part):
    first_key = jax.random.fold_in(key, 0)
    spread = 0.5 / C ** 0.5
    noise = jax.random.truncated_normal(first_key, -4.0, 4.0, (BINS, 2, C, C), jnp.float32) * spread
    diagonal = jnp.eye(C, dtype=jnp.float32) * 0.6
    which_part = jnp.arange(2, dtype=jnp.int32)
    real_only = (which_part == 0).astype(jnp.float32)
    return (noise + real_only[None, :, None, None] * diagonal[None, None]).astype(jnp.bfloat16)


def block_scale(stream_key, extent, pieces, least, largest):
    gain, own = 1.0, jax.random.fold_in(stream_key, 6)
    for dim, blocks in pieces:
        heights = jnp.exp(jax.random.uniform(jax.random.fold_in(own, dim), (blocks,), jnp.float32, least / len(pieces), largest / len(pieces)))
        gain = gain * jnp.repeat(heights, extent[dim] // blocks).reshape([-1 if axis == dim else 1 for axis in range(len(extent))])
    return gain


def bell_draw(rng, extent, scale, most, cuts=(), held_as=jnp.bfloat16):
    loudness = block_scale(rng, extent, cuts, -0.22, 0.18) if cuts else 1.0
    entries = jax.random.normal(rng, extent, jnp.float32) * scale * loudness
    return jnp.minimum(jnp.maximum(entries, -most), most).astype(held_as)


def setup_inputs(seed: int = 0) -> dict:
    key_list = jax.random.split(jax.random.key(seed), 6)
    output_grad = bell_draw(key_list[0], (IMAGES, C, PIX), 1.0, 6.0, ((0, 512),))
    layer_input = bell_draw(key_list[1], (IMAGES, C, PIX), 1.0, 6.0, ((0, 512),))
    counts = draw_counts(jax.random.fold_in(key_list[5], 71), 0)
    bin_order = draw_bin_order(jax.random.fold_in(key_list[5], 71), 0)
    inverse_factor = draw_inverse_factor(jax.random.fold_in(key_list[5], 71), 0)
    return {"output_grad": output_grad, "layer_input": layer_input, "counts": counts, "bin_order": bin_order, "inverse_factor": inverse_factor}


def dft_table(bin_order, grid_side):
    pixel_index = jnp.arange(grid_side * grid_side, dtype=jnp.int32)
    row_pos = pixel_index // grid_side
    col_pos = pixel_index % grid_side
    freq_u = bin_order // grid_side
    freq_v = bin_order % grid_side
    phase_turns = (row_pos[:, None] * freq_u[None, :] + col_pos[:, None] * freq_v[None, :]) % grid_side
    phase_angle = phase_turns.astype(jnp.float32) * (2.0 * math.pi / grid_side)
    both_parts = jnp.stack([jnp.cos(phase_angle), -jnp.sin(phase_angle)], axis=2) / grid_side
    return both_parts.reshape(grid_side * grid_side, -1).astype(jnp.bfloat16)

def tap_phases(bin_order, grid_side):
    offsets = jnp.arange(9, dtype=jnp.int32)
    shift_y = offsets // 3 - 1
    shift_x = offsets % 3 - 1
    freq_u = bin_order // grid_side
    freq_v = bin_order % grid_side
    phase_turns = (freq_u[:, None] * shift_y[None, :] + freq_v[:, None] * shift_x[None, :]) % grid_side
    phase_angle = phase_turns.astype(jnp.float32) * (2.0 * math.pi / grid_side)
    return (jnp.cos(phase_angle), jnp.sin(phase_angle))

def reference(output_grad, layer_input, counts, bin_order, inverse_factor):
    shard_count = counts.shape[0]
    image_count = output_grad.shape[0]
    slot_count = image_count // shard_count
    channels = output_grad.shape[1]
    bin_count = bin_order.shape[0]
    bins_table = dft_table(bin_order, GRID).astype(jnp.float32)
    live_mask = (jnp.arange(slot_count, dtype=jnp.int32)[None, :] < counts[:, None]).astype(jnp.bfloat16)
    grad_shards = output_grad.reshape(shard_count, slot_count, channels, GRID * GRID)
    input_shards = layer_input.reshape(shard_count, slot_count, channels, GRID * GRID)

    def shard_spectra(bundle):
        grad_block, input_block, mask_row = bundle

        def spectrum(images):
            masked = (images * mask_row[:, None, None]).astype(jnp.float32)
            return jnp.einsum('scp,pk->skc', masked, bins_table).astype(jnp.bfloat16)
        return (spectrum(grad_block), spectrum(input_block))
    grad_spec, input_spec = lax.map(shard_spectra, (grad_shards, input_shards, live_mask))
    grad_bins = jnp.transpose(grad_spec.reshape(image_count, bin_count, 2, channels), (1, 0, 2, 3))
    input_bins = jnp.transpose(input_spec.reshape(image_count, bin_count, 2, channels), (1, 0, 2, 3))
    cos_all, sin_all = tap_phases(bin_order, GRID)
    gram_scale = 1.0 / math.sqrt(image_count)

    def per_bin(tap_total, bundle):
        grad_bin, input_bin, factor, cos_row, sin_row = bundle
        grad_real = grad_bin[:, 0]
        grad_imag = grad_bin[:, 1]
        input_real = input_bin[:, 0]
        input_imag = input_bin[:, 1]
        factor_real = factor[0]
        factor_imag = factor[1]
        back_real = 2.0 * (jnp.dot(grad_real, factor_real, preferred_element_type=jnp.float32) + jnp.dot(grad_imag, factor_imag, preferred_element_type=jnp.float32)) - grad_real.astype(jnp.float32)
        back_imag = 2.0 * (jnp.dot(grad_imag, factor_real, preferred_element_type=jnp.float32) - jnp.dot(grad_real, factor_imag, preferred_element_type=jnp.float32)) - grad_imag.astype(jnp.float32)
        back_both = jnp.stack([back_real, back_imag], axis=1).astype(jnp.bfloat16)
        gram_real = (jnp.dot(grad_real.T, input_real, preferred_element_type=jnp.float32) + jnp.dot(grad_imag.T, input_imag, preferred_element_type=jnp.float32)) * gram_scale
        gram_imag = (jnp.dot(grad_imag.T, input_real, preferred_element_type=jnp.float32) - jnp.dot(grad_real.T, input_imag, preferred_element_type=jnp.float32)) * gram_scale
        gram_real = gram_real.astype(jnp.bfloat16)
        gram_imag = gram_imag.astype(jnp.bfloat16)
        half_real = (jnp.dot(gram_real, factor_real.T, preferred_element_type=jnp.float32) + jnp.dot(gram_imag, factor_imag.T, preferred_element_type=jnp.float32)).astype(jnp.bfloat16)
        half_imag = (jnp.dot(gram_imag, factor_real.T, preferred_element_type=jnp.float32) - jnp.dot(gram_real, factor_imag.T, preferred_element_type=jnp.float32)).astype(jnp.bfloat16)
        full_real = -2.0 * (jnp.dot(factor_real.T, half_real, preferred_element_type=jnp.float32) + jnp.dot(factor_imag.T, half_imag, preferred_element_type=jnp.float32))
        full_imag = -2.0 * (jnp.dot(factor_real.T, half_imag, preferred_element_type=jnp.float32) - jnp.dot(factor_imag.T, half_real, preferred_element_type=jnp.float32))
        skew_real = full_real - full_real.T
        skew_imag = full_imag + full_imag.T
        tap_total = tap_total + cos_row[:, None, None] * skew_real[None] - sin_row[:, None, None] * skew_imag[None]
        return (tap_total, back_both)
    start_taps = jnp.zeros((TAPS, channels, channels), jnp.float32)
    tap_total, back_all = lax.scan(per_bin, start_taps, (grad_bins, input_bins, inverse_factor, cos_all, sin_all))
    tap_grad = tap_total / math.sqrt(bin_count)
    input_spectra_grad = jnp.transpose(back_all, (1, 0, 2, 3)).reshape(image_count, 2 * bin_count, channels)
    return (input_spectra_grad, tap_grad)
```

```python
import math

import jax
import jax.numpy as jnp
from jax import lax
from jax.sharding import PartitionSpec as P

GRID = 32


def dft_table(bin_order, grid_side):
    pixel_index = jnp.arange(grid_side * grid_side, dtype=jnp.int32)
    row_pos = pixel_index // grid_side
    col_pos = pixel_index % grid_side
    freq_u = bin_order // grid_side
    freq_v = bin_order % grid_side
    phase_turns = (
        row_pos[:, None] * freq_u[None, :] + col_pos[:, None] * freq_v[None, :]
    ) % grid_side
    phase_angle = phase_turns.astype(jnp.float32) * (2.0 * math.pi / grid_side)
    both_parts = jnp.stack([jnp.cos(phase_angle), -jnp.sin(phase_angle)], axis=2) / grid_side
    return both_parts.reshape(grid_side * grid_side, -1).astype(jnp.bfloat16)


def tap_phases(bin_order, grid_side):
    offsets = jnp.arange(9, dtype=jnp.int32)
    shift_y = offsets // 3 - 1
    shift_x = offsets % 3 - 1
    freq_u = bin_order // grid_side
    freq_v = bin_order % grid_side
    phase_turns = (
        freq_u[:, None] * shift_y[None, :] + freq_v[:, None] * shift_x[None, :]
    ) % grid_side
    phase_angle = phase_turns.astype(jnp.float32) * (2.0 * math.pi / grid_side)
    return (jnp.cos(phase_angle), jnp.sin(phase_angle))


def left_product(factor_real, factor_imag, half_real, half_imag):
    full_real = -2.0 * (
        jnp.einsum("bkr,bkc->brc", factor_real, half_real, preferred_element_type=jnp.float32)
        + jnp.einsum("bkr,bkc->brc", factor_imag, half_imag, preferred_element_type=jnp.float32)
    )
    full_imag = -2.0 * (
        jnp.einsum("bkr,bkc->brc", factor_real, half_imag, preferred_element_type=jnp.float32)
        - jnp.einsum("bkr,bkc->brc", factor_imag, half_real, preferred_element_type=jnp.float32)
    )
    return (full_real, full_imag)


def local(output_grad, layer_input, counts, bin_order, inverse_factor):
    slot_count, channels, pixels = output_grad.shape
    freq_devices = lax.axis_size("freq")
    data_devices = lax.axis_size("dp")
    bins_local = inverse_factor.shape[0]
    total_bins = bin_order.shape[0]
    live_mask = (jnp.arange(slot_count, dtype=jnp.int32) < counts[0]).astype(jnp.bfloat16)
    bins_table = dft_table(bin_order, GRID)

    def spectrum(images):
        masked = images * live_mask[:, None, None]
        return jnp.einsum(
            "scp,pk->skc", masked, bins_table, preferred_element_type=jnp.float32
        ).astype(jnp.bfloat16)

    grad_spec = spectrum(output_grad)
    input_spec = spectrum(layer_input)
    grad_recv, input_recv = (
        lax.all_to_all(grad_spec, "freq", split_axis=1, concat_axis=0, tiled=True),
        lax.all_to_all(input_spec, "freq", split_axis=1, concat_axis=0, tiled=True),
    )
    image_rows = grad_recv.shape[0]
    grad_parts = grad_recv.reshape(image_rows, bins_local, 2, channels)
    input_parts = input_recv.reshape(image_rows, bins_local, 2, channels)
    grad_real = grad_parts[:, :, 0]
    grad_imag = grad_parts[:, :, 1]
    input_real = input_parts[:, :, 0]
    input_imag = input_parts[:, :, 1]
    factor_real = inverse_factor[:, 0]
    factor_imag = inverse_factor[:, 1]
    back_real = 2.0 * (
        jnp.einsum("ibr,brc->ibc", grad_real, factor_real, preferred_element_type=jnp.float32)
        + jnp.einsum("ibr,brc->ibc", grad_imag, factor_imag, preferred_element_type=jnp.float32)
    ) - grad_real.astype(jnp.float32)
    back_imag = 2.0 * (
        jnp.einsum("ibr,brc->ibc", grad_imag, factor_real, preferred_element_type=jnp.float32)
        - jnp.einsum("ibr,brc->ibc", grad_real, factor_imag, preferred_element_type=jnp.float32)
    ) - grad_imag.astype(jnp.float32)
    back_both = (
        jnp.stack([back_real, back_imag], axis=2)
        .astype(jnp.bfloat16)
        .reshape(image_rows, 2 * bins_local, channels)
    )
    returned = lax.all_to_all(back_both, "freq", split_axis=0, concat_axis=1, tiled=True)
    gram_scale = 1.0 / math.sqrt(data_devices * freq_devices * slot_count)
    gram_real = (
        jnp.einsum("ibr,ibc->brc", grad_real, input_real, preferred_element_type=jnp.float32)
        + jnp.einsum("ibr,ibc->brc", grad_imag, input_imag, preferred_element_type=jnp.float32)
    ) * gram_scale
    gram_imag = (
        jnp.einsum("ibr,ibc->brc", grad_imag, input_real, preferred_element_type=jnp.float32)
        - jnp.einsum("ibr,ibc->brc", grad_real, input_imag, preferred_element_type=jnp.float32)
    ) * gram_scale
    gram_local = jnp.stack([gram_real, gram_imag], axis=1)
    gram_matrix = lax.psum(gram_local, "dp").astype(jnp.bfloat16)
    summed_real = gram_matrix[:, 0]
    summed_imag = gram_matrix[:, 1]
    half_real = (
        jnp.einsum("brk,bck->brc", summed_real, factor_real, preferred_element_type=jnp.float32)
        + jnp.einsum("brk,bck->brc", summed_imag, factor_imag, preferred_element_type=jnp.float32)
    ).astype(jnp.bfloat16)
    half_imag = (
        jnp.einsum("brk,bck->brc", summed_imag, factor_real, preferred_element_type=jnp.float32)
        - jnp.einsum("brk,bck->brc", summed_real, factor_imag, preferred_element_type=jnp.float32)
    ).astype(jnp.bfloat16)
    row_share = channels // data_devices
    row_start = lax.axis_index("dp") * row_share
    full_real, full_imag = left_product(factor_real, factor_imag, half_real, half_imag)
    skew_real = full_real - jnp.swapaxes(full_real, 1, 2)
    skew_imag = full_imag + jnp.swapaxes(full_imag, 1, 2)
    skew_real = lax.dynamic_slice_in_dim(skew_real, row_start, row_share, 1)
    skew_imag = lax.dynamic_slice_in_dim(skew_imag, row_start, row_share, 1)
    local_bins = lax.dynamic_slice_in_dim(
        bin_order, lax.axis_index("freq") * bins_local, bins_local
    )
    cos_local, sin_local = tap_phases(local_bins, GRID)
    tap_partial = jnp.sum(
        cos_local[:, :, None, None] * skew_real[:, None]
        - sin_local[:, :, None, None] * skew_imag[:, None],
        axis=0,
    )
    tap_partial = tap_partial / math.sqrt(total_bins)
    col_share = channels // freq_devices
    tap_pieces = jnp.transpose(
        tap_partial.reshape(tap_partial.shape[0], row_share, freq_devices, col_share), (2, 0, 1, 3)
    )
    tap_pieces = lax.all_to_all(tap_pieces, "freq", split_axis=0, concat_axis=0, tiled=True)
    tap_grad = jnp.sum(tap_pieces, axis=0)
    return (returned, tap_grad)


def solution(mesh):
    return jax.shard_map(
        local,
        mesh=mesh,
        in_specs=(
            P(("dp", "freq"), None, None),
            P(("dp", "freq"), None, None),
            P(("dp", "freq")),
            P(),
            P("freq", None, None, None),
        ),
        out_specs=(P(("dp", "freq"), None, None), P(None, "dp", "freq")),
        check_vma=False,
    )
```

```python
import math

import jax
import jax.numpy as jnp
from jax import lax
from jax.sharding import PartitionSpec as P

GRID = 32


def dft_table(bin_order, grid_side):
    pixel_index = jnp.arange(grid_side * grid_side, dtype=jnp.int32)
    row_pos = pixel_index // grid_side
    col_pos = pixel_index % grid_side
    freq_u = bin_order // grid_side
    freq_v = bin_order % grid_side
    phase_turns = (
        row_pos[:, None] * freq_u[None, :] + col_pos[:, None] * freq_v[None, :]
    ) % grid_side
    phase_angle = phase_turns.astype(jnp.float32) * (2.0 * math.pi / grid_side)
    both_parts = jnp.stack([jnp.cos(phase_angle), -jnp.sin(phase_angle)], axis=2) / grid_side
    return both_parts.reshape(grid_side * grid_side, -1).astype(jnp.bfloat16)


def tap_phases(bin_order, grid_side):
    offsets = jnp.arange(9, dtype=jnp.int32)
    shift_y = offsets // 3 - 1
    shift_x = offsets % 3 - 1
    freq_u = bin_order // grid_side
    freq_v = bin_order % grid_side
    phase_turns = (
        freq_u[:, None] * shift_y[None, :] + freq_v[:, None] * shift_x[None, :]
    ) % grid_side
    phase_angle = phase_turns.astype(jnp.float32) * (2.0 * math.pi / grid_side)
    return (jnp.cos(phase_angle), jnp.sin(phase_angle))


def left_product(factor_real, factor_imag, half_real, half_imag):
    full_real = -2.0 * (
        jnp.einsum("bkr,bkc->brc", factor_real, half_real, preferred_element_type=jnp.float32)
        + jnp.einsum("bkr,bkc->brc", factor_imag, half_imag, preferred_element_type=jnp.float32)
    )
    full_imag = -2.0 * (
        jnp.einsum("bkr,bkc->brc", factor_real, half_imag, preferred_element_type=jnp.float32)
        - jnp.einsum("bkr,bkc->brc", factor_imag, half_real, preferred_element_type=jnp.float32)
    )
    return (full_real, full_imag)


def local(output_grad, layer_input, counts, bin_order, inverse_factor):
    slot_count, channels, pixels = output_grad.shape
    freq_devices = lax.axis_size("freq")
    data_devices = lax.axis_size("dp")
    bins_local = inverse_factor.shape[0]
    total_bins = bin_order.shape[0]
    live_mask = (jnp.arange(slot_count, dtype=jnp.int32) < counts[0]).astype(jnp.bfloat16)
    bins_table = dft_table(bin_order, GRID)

    def spectrum(images):
        masked = images * live_mask[:, None, None]
        return jnp.einsum(
            "scp,pk->skc", masked, bins_table, preferred_element_type=jnp.float32
        ).astype(jnp.bfloat16)

    grad_spec = spectrum(output_grad)
    input_spec = spectrum(layer_input)
    grad_recv, input_recv = (
        lax.all_to_all(grad_spec, "freq", split_axis=1, concat_axis=0, tiled=True),
        lax.all_to_all(input_spec, "freq", split_axis=1, concat_axis=0, tiled=True),
    )
    image_rows = grad_recv.shape[0]
    grad_parts = grad_recv.reshape(image_rows, bins_local, 2, channels)
    input_parts = input_recv.reshape(image_rows, bins_local, 2, channels)
    grad_real = grad_parts[:, :, 0]
    grad_imag = grad_parts[:, :, 1]
    input_real = input_parts[:, :, 0]
    input_imag = input_parts[:, :, 1]
    factor_real = inverse_factor[:, 0]
    factor_imag = inverse_factor[:, 1]
    back_real = 2.0 * (
        jnp.einsum("ibr,brc->ibc", grad_real, factor_real, preferred_element_type=jnp.float32)
        + jnp.einsum("ibr,brc->ibc", grad_imag, factor_imag, preferred_element_type=jnp.float32)
    ) - grad_real.astype(jnp.float32)
    back_imag = 2.0 * (
        jnp.einsum("ibr,brc->ibc", grad_imag, factor_real, preferred_element_type=jnp.float32)
        - jnp.einsum("ibr,brc->ibc", grad_real, factor_imag, preferred_element_type=jnp.float32)
    ) - grad_imag.astype(jnp.float32)
    back_both = (
        jnp.stack([back_real, back_imag], axis=2)
        .astype(jnp.bfloat16)
        .reshape(image_rows, 2 * bins_local, channels)
    )
    returned = lax.all_to_all(back_both, "freq", split_axis=0, concat_axis=1, tiled=True)
    gram_scale = 1.0 / math.sqrt(data_devices * freq_devices * slot_count)
    gram_real = (
        jnp.einsum("ibr,ibc->brc", grad_real, input_real, preferred_element_type=jnp.float32)
        + jnp.einsum("ibr,ibc->brc", grad_imag, input_imag, preferred_element_type=jnp.float32)
    ) * gram_scale
    gram_imag = (
        jnp.einsum("ibr,ibc->brc", grad_imag, input_real, preferred_element_type=jnp.float32)
        - jnp.einsum("ibr,ibc->brc", grad_real, input_imag, preferred_element_type=jnp.float32)
    ) * gram_scale
    summed_real = gram_real.astype(jnp.bfloat16)
    summed_imag = gram_imag.astype(jnp.bfloat16)
    half_real = (
        jnp.einsum("brk,bck->brc", summed_real, factor_real, preferred_element_type=jnp.float32)
        + jnp.einsum("brk,bck->brc", summed_imag, factor_imag, preferred_element_type=jnp.float32)
    ).astype(jnp.bfloat16)
    half_imag = (
        jnp.einsum("brk,bck->brc", summed_imag, factor_real, preferred_element_type=jnp.float32)
        - jnp.einsum("brk,bck->brc", summed_real, factor_imag, preferred_element_type=jnp.float32)
    ).astype(jnp.bfloat16)
    full_real, full_imag = left_product(factor_real, factor_imag, half_real, half_imag)
    local_bins = lax.dynamic_slice_in_dim(
        bin_order, lax.axis_index("freq") * bins_local, bins_local
    )
    cos_local, sin_local = tap_phases(local_bins, GRID)
    tap_scale = 1.0 / math.sqrt(total_bins)
    phased = jnp.einsum(
        "bt,brc->trc", cos_local * tap_scale, full_real, preferred_element_type=jnp.float32
    ) - jnp.einsum(
        "bt,brc->trc", sin_local * tap_scale, full_imag, preferred_element_type=jnp.float32
    )
    tap_partial = phased - jnp.swapaxes(phased[::-1], 1, 2)
    taps = tap_partial.shape[0]
    col_share = channels // freq_devices
    row_share = channels // data_devices
    col_pieces = jnp.transpose(
        tap_partial.astype(jnp.bfloat16).reshape(taps, channels, freq_devices, col_share),
        (2, 0, 1, 3),
    )
    col_pieces = lax.all_to_all(col_pieces, "freq", split_axis=0, concat_axis=0, tiled=True)
    col_sum = jnp.sum(col_pieces.astype(jnp.float32), axis=0)
    row_pieces = jnp.transpose(
        col_sum.astype(jnp.bfloat16).reshape(taps, data_devices, row_share, col_share),
        (1, 0, 2, 3),
    )
    row_pieces = lax.all_to_all(row_pieces, "dp", split_axis=0, concat_axis=0, tiled=True)
    tap_grad = jnp.sum(row_pieces.astype(jnp.float32), axis=0)
    return (returned, tap_grad)


def solution(mesh):
    return jax.shard_map(
        local,
        mesh=mesh,
        in_specs=(
            P(("dp", "freq"), None, None),
            P(("dp", "freq"), None, None),
            P(("dp", "freq")),
            P(),
            P("freq", None, None, None),
        ),
        out_specs=(P(("dp", "freq"), None, None), P(None, "dp", "freq")),
        check_vma=False,
    )
```

```python
import math

import jax
import jax.numpy as jnp
from jax import lax
from jax.sharding import PartitionSpec as P

GRID = 32


def dft_table(bin_order, grid_side):
    pixel_index = jnp.arange(grid_side * grid_side, dtype=jnp.int32)
    row_pos = pixel_index // grid_side
    col_pos = pixel_index % grid_side
    freq_u = bin_order // grid_side
    freq_v = bin_order % grid_side
    phase_turns = (
        row_pos[:, None] * freq_u[None, :] + col_pos[:, None] * freq_v[None, :]
    ) % grid_side
    phase_angle = phase_turns.astype(jnp.float32) * (2.0 * math.pi / grid_side)
    both_parts = jnp.stack([jnp.cos(phase_angle), -jnp.sin(phase_angle)], axis=2) / grid_side
    return both_parts.reshape(grid_side * grid_side, -1).astype(jnp.bfloat16)


def tap_phases(bin_order, grid_side):
    offsets = jnp.arange(9, dtype=jnp.int32)
    shift_y = offsets // 3 - 1
    shift_x = offsets % 3 - 1
    freq_u = bin_order // grid_side
    freq_v = bin_order % grid_side
    phase_turns = (
        freq_u[:, None] * shift_y[None, :] + freq_v[:, None] * shift_x[None, :]
    ) % grid_side
    phase_angle = phase_turns.astype(jnp.float32) * (2.0 * math.pi / grid_side)
    return (jnp.cos(phase_angle), jnp.sin(phase_angle))


def local(output_grad, layer_input, counts, bin_order, inverse_factor):
    slot_count, channels, pixels = output_grad.shape
    freq_devices = lax.axis_size("freq")
    data_devices = lax.axis_size("dp")
    bins_local = inverse_factor.shape[0]
    total_bins = bin_order.shape[0]
    live_mask = (jnp.arange(slot_count, dtype=jnp.int32) < counts[0]).astype(jnp.bfloat16)
    bins_table = dft_table(bin_order, GRID)

    def spectrum(images):
        masked = images * live_mask[:, None, None]
        return jnp.einsum(
            "scp,pk->skc", masked, bins_table, preferred_element_type=jnp.float32
        ).astype(jnp.bfloat16)

    both_spec = jnp.stack([spectrum(output_grad), spectrum(layer_input)], axis=0)
    both_recv = lax.all_to_all(both_spec, "freq", split_axis=2, concat_axis=1, tiled=True)
    image_rows = both_recv.shape[1]
    parts = both_recv.reshape(2, image_rows, bins_local, 2, channels)
    grad_real = parts[0, :, :, 0]
    grad_imag = parts[0, :, :, 1]
    input_real = parts[1, :, :, 0]
    input_imag = parts[1, :, :, 1]
    factor_real = inverse_factor[:, 0]
    factor_imag = inverse_factor[:, 1]
    f32 = jnp.float32

    def mm(x, p, eq):
        return jnp.einsum(eq, x, p, preferred_element_type=f32)

    u_real = mm(grad_real, factor_real, "ibr,brc->ibc") + mm(grad_imag, factor_imag, "ibr,brc->ibc")
    u_imag = mm(grad_imag, factor_real, "ibr,brc->ibc") - mm(grad_real, factor_imag, "ibr,brc->ibc")
    back_real = 2.0 * u_real - grad_real.astype(f32)
    back_imag = 2.0 * u_imag - grad_imag.astype(f32)
    back_both = (
        jnp.stack([back_real, back_imag], axis=2)
        .astype(jnp.bfloat16)
        .reshape(image_rows, 2 * bins_local, channels)
    )
    returned = lax.all_to_all(back_both, "freq", split_axis=0, concat_axis=1, tiled=True)
    v_real = mm(input_real, factor_real, "ibk,bck->ibc") - mm(input_imag, factor_imag, "ibk,bck->ibc")
    v_imag = mm(input_real, factor_imag, "ibk,bck->ibc") + mm(input_imag, factor_real, "ibk,bck->ibc")
    local_bins = lax.dynamic_slice_in_dim(
        bin_order, lax.axis_index("freq") * bins_local, bins_local
    )
    cos_local, sin_local = tap_phases(local_bins, GRID)
    cos_t = cos_local.T[:, None, :, None]
    sin_t = sin_local.T[:, None, :, None]
    ur = u_real[None]
    ui = u_imag[None]
    z_t = jnp.stack([cos_t * ur - sin_t * ui, cos_t * ui + sin_t * ur], axis=1).astype(jnp.bfloat16)
    w_t = jnp.stack([cos_t * ur + sin_t * ui, cos_t * ui - sin_t * ur], axis=1).astype(jnp.bfloat16)
    y_all = jnp.stack([v_real, v_imag], axis=0).astype(jnp.bfloat16)
    taps = z_t.shape[0]
    col_share = channels // freq_devices
    row_share = channels // data_devices
    y_cols = y_all.reshape(2, image_rows, bins_local, freq_devices, col_share)
    w_cols = w_t.reshape(taps, 2, image_rows, bins_local, freq_devices, col_share)
    first = jnp.einsum("teibr,eibfc->ftrc", z_t, y_cols, preferred_element_type=f32)
    second = jnp.einsum("eibr,teibfc->ftrc", y_all, w_cols, preferred_element_type=f32)
    gram_scale = 1.0 / math.sqrt(data_devices * freq_devices * slot_count)
    tap_scale = 2.0 * gram_scale / math.sqrt(total_bins)
    col_pieces = ((second - first) * tap_scale).astype(jnp.bfloat16)
    col_pieces = lax.all_to_all(col_pieces, "freq", split_axis=0, concat_axis=0, tiled=True)
    col_sum = jnp.sum(col_pieces.astype(f32), axis=0)
    row_pieces = jnp.transpose(
        col_sum.reshape(taps, data_devices, row_share, col_share), (1, 0, 2, 3)
    )
    row_pieces = lax.all_to_all(row_pieces, "dp", split_axis=0, concat_axis=0, tiled=True)
    tap_grad = jnp.sum(row_pieces, axis=0)
    return (returned, tap_grad)


def solution(mesh):
    return jax.shard_map(
        local,
        mesh=mesh,
        in_specs=(
            P(("dp", "freq"), None, None),
            P(("dp", "freq"), None, None),
            P(("dp", "freq")),
            P(),
            P("freq", None, None, None),
        ),
        out_specs=(P(("dp", "freq"), None, None), P(None, "dp", "freq")),
        check_vma=False,
    )
```

```python
import math

import jax
import jax.numpy as jnp
from jax import lax
from jax.sharding import Mesh, PartitionSpec as P

GRID = 32


def dft_table(bin_order, grid_side):
    pixel_index = jnp.arange(grid_side * grid_side, dtype=jnp.int32)
    row_pos = pixel_index // grid_side
    col_pos = pixel_index % grid_side
    freq_u = bin_order // grid_side
    freq_v = bin_order % grid_side
    phase_turns = (
        row_pos[:, None] * freq_u[None, :] + col_pos[:, None] * freq_v[None, :]
    ) % grid_side
    phase_angle = phase_turns.astype(jnp.float32) * (2.0 * math.pi / grid_side)
    both_parts = jnp.stack([jnp.cos(phase_angle), -jnp.sin(phase_angle)], axis=2) / grid_side
    return both_parts.reshape(grid_side * grid_side, -1).astype(jnp.bfloat16)


def tap_phases(bin_order, grid_side):
    offsets = jnp.arange(9, dtype=jnp.int32)
    shift_y = offsets // 3 - 1
    shift_x = offsets % 3 - 1
    freq_u = bin_order // grid_side
    freq_v = bin_order % grid_side
    phase_turns = (
        freq_u[:, None] * shift_y[None, :] + freq_v[:, None] * shift_x[None, :]
    ) % grid_side
    phase_angle = phase_turns.astype(jnp.float32) * (2.0 * math.pi / grid_side)
    return (jnp.cos(phase_angle), jnp.sin(phase_angle))


def local(output_grad, layer_input, counts, bin_order, inverse_factor):
    slot_count, channels, pixels = output_grad.shape
    freq_devices = lax.axis_size("freq")
    bins_local = inverse_factor.shape[0]
    total_bins = bin_order.shape[0]
    live_mask = (jnp.arange(slot_count, dtype=jnp.int32) < counts[0]).astype(jnp.bfloat16)
    bins_table = dft_table(bin_order, GRID)

    def spectrum(images):
        masked = images * live_mask[:, None, None]
        return jnp.einsum(
            "scp,pk->skc", masked, bins_table, preferred_element_type=jnp.float32
        ).astype(jnp.bfloat16)

    both_spec = jnp.stack([spectrum(output_grad), spectrum(layer_input)], axis=0)
    both_recv = lax.all_to_all(both_spec, "freq", split_axis=2, concat_axis=1, tiled=True)
    image_rows = both_recv.shape[1]
    parts = both_recv.reshape(2, image_rows, bins_local, 2, channels)
    grad_real = parts[0, :, :, 0]
    grad_imag = parts[0, :, :, 1]
    input_real = parts[1, :, :, 0]
    input_imag = parts[1, :, :, 1]
    factor_real = inverse_factor[:, 0]
    factor_imag = inverse_factor[:, 1]
    f32 = jnp.float32

    def mm(x, p, eq):
        return jnp.einsum(eq, x, p, preferred_element_type=f32)

    u_real = mm(grad_real, factor_real, "ibr,brc->ibc") + mm(grad_imag, factor_imag, "ibr,brc->ibc")
    u_imag = mm(grad_imag, factor_real, "ibr,brc->ibc") - mm(grad_real, factor_imag, "ibr,brc->ibc")
    back_real = 2.0 * u_real - grad_real.astype(f32)
    back_imag = 2.0 * u_imag - grad_imag.astype(f32)
    back_both = (
        jnp.stack([back_real, back_imag], axis=2)
        .astype(jnp.bfloat16)
        .reshape(image_rows, 2 * bins_local, channels)
    )
    returned = lax.all_to_all(back_both, "freq", split_axis=0, concat_axis=1, tiled=True)
    v_real = mm(input_real, factor_real, "ibk,bck->ibc") - mm(input_imag, factor_imag, "ibk,bck->ibc")
    v_imag = mm(input_real, factor_imag, "ibk,bck->ibc") + mm(input_imag, factor_real, "ibk,bck->ibc")
    local_bins = lax.dynamic_slice_in_dim(
        bin_order, lax.axis_index("freq") * bins_local, bins_local
    )
    cos_local, sin_local = tap_phases(local_bins, GRID)
    cos_t = cos_local.T[:, None, :, None]
    sin_t = sin_local.T[:, None, :, None]
    ur = u_real[None]
    ui = u_imag[None]
    z_t = jnp.stack([cos_t * ur - sin_t * ui, cos_t * ui + sin_t * ur], axis=1).astype(jnp.bfloat16)
    w_t = jnp.stack([cos_t * ur + sin_t * ui, cos_t * ui - sin_t * ur], axis=1).astype(jnp.bfloat16)
    y_all = jnp.stack([v_real, v_imag], axis=0).astype(jnp.bfloat16)
    taps = z_t.shape[0]
    z_devices = lax.axis_size("z")
    core_devices = lax.axis_size("c")
    col_share = channels // freq_devices
    row_share = channels // (z_devices * core_devices)
    def core_major(x):
        lead = x.shape[:-1]
        x = x.reshape(lead + (z_devices, core_devices, row_share))
        x = jnp.swapaxes(x, -3, -2)
        return x.reshape(lead + (core_devices, z_devices * row_share))

    z_rows = core_major(z_t)
    y_rows = core_major(y_all)
    y_cols = y_all.reshape(2, image_rows, bins_local, freq_devices, col_share)
    w_cols = w_t.reshape(taps, 2, image_rows, bins_local, freq_devices, col_share)
    first = jnp.einsum("teibCr,eibfk->Cftrk", z_rows, y_cols, preferred_element_type=f32)
    second = jnp.einsum("eibCr,teibfk->Cftrk", y_rows, w_cols, preferred_element_type=f32)
    gram_scale = 1.0 / math.sqrt(z_devices * core_devices * freq_devices * slot_count)
    tap_scale = 2.0 * gram_scale / math.sqrt(total_bins)
    chip_pieces = (second - first) * tap_scale
    chip_pieces = lax.all_to_all(chip_pieces, "c", split_axis=0, concat_axis=0, tiled=True)
    col_pieces = jnp.sum(chip_pieces, axis=0).astype(jnp.bfloat16)
    col_pieces = lax.all_to_all(col_pieces, "freq", split_axis=0, concat_axis=0, tiled=True)
    row_pieces = jnp.sum(col_pieces.astype(f32), axis=0)
    row_pieces = jnp.transpose(
        row_pieces.reshape(taps, z_devices, row_share, col_share), (1, 0, 2, 3)
    )
    row_pieces = lax.all_to_all(row_pieces, "z", split_axis=0, concat_axis=0, tiled=True)
    tap_grad = jnp.sum(row_pieces, axis=0)
    return (returned, tap_grad)


def solution(mesh):
    cores = 2
    chips = Mesh(
        mesh.devices.reshape(mesh.shape["dp"] // cores, cores, mesh.shape["freq"]),
        ("z", "c", "freq"),
    )
    return jax.shard_map(
        local,
        mesh=chips,
        in_specs=(
            P(("z", "c", "freq"), None, None),
            P(("z", "c", "freq"), None, None),
            P(("z", "c", "freq")),
            P(),
            P("freq", None, None, None),
        ),
        out_specs=(P(("z", "c", "freq"), None, None), P(None, ("z", "c"), "freq")),
        check_vma=False,
    )
```

```python
import math

import jax
import jax.numpy as jnp
from jax import lax
from jax.sharding import PartitionSpec as P

GRID = 32


def dft_table(bin_order, grid_side):
    pixel_index = jnp.arange(grid_side * grid_side, dtype=jnp.int32)
    row_pos = pixel_index // grid_side
    col_pos = pixel_index % grid_side
    freq_u = bin_order // grid_side
    freq_v = bin_order % grid_side
    phase_turns = (
        row_pos[:, None] * freq_u[None, :] + col_pos[:, None] * freq_v[None, :]
    ) % grid_side
    phase_angle = phase_turns.astype(jnp.float32) * (2.0 * math.pi / grid_side)
    both_parts = jnp.stack([jnp.cos(phase_angle), -jnp.sin(phase_angle)], axis=2) / grid_side
    return both_parts.reshape(grid_side * grid_side, -1).astype(jnp.bfloat16)


def tap_phases(bin_order, grid_side):
    offsets = jnp.arange(9, dtype=jnp.int32)
    shift_y = offsets // 3 - 1
    shift_x = offsets % 3 - 1
    freq_u = bin_order // grid_side
    freq_v = bin_order % grid_side
    phase_turns = (
        freq_u[:, None] * shift_y[None, :] + freq_v[:, None] * shift_x[None, :]
    ) % grid_side
    phase_angle = phase_turns.astype(jnp.float32) * (2.0 * math.pi / grid_side)
    return (jnp.cos(phase_angle), jnp.sin(phase_angle))


def local(output_grad, layer_input, counts, bin_order, inverse_factor):
    slot_count, channels, pixels = output_grad.shape
    freq_devices = lax.axis_size("freq")
    data_devices = lax.axis_size("dp")
    bins_local = inverse_factor.shape[0]
    total_bins = bin_order.shape[0]
    live_mask = (jnp.arange(slot_count, dtype=jnp.int32) < counts[0]).astype(jnp.bfloat16)
    bins_table = dft_table(bin_order, GRID)

    def spectrum(images):
        masked = images * live_mask[:, None, None]
        return jnp.einsum(
            "scp,pk->skc", masked, bins_table, preferred_element_type=jnp.float32
        ).astype(jnp.bfloat16)

    both_spec = jnp.stack([spectrum(output_grad), spectrum(layer_input)], axis=0)
    both_recv = lax.all_to_all(both_spec, "freq", split_axis=2, concat_axis=1, tiled=True)
    image_rows = both_recv.shape[1]
    parts = both_recv.reshape(2, image_rows, bins_local, 2, channels)
    grad_real = parts[0, :, :, 0]
    grad_imag = parts[0, :, :, 1]
    input_real = parts[1, :, :, 0]
    input_imag = parts[1, :, :, 1]
    factor_real = inverse_factor[:, 0]
    factor_imag = inverse_factor[:, 1]
    f32 = jnp.float32

    def mm(x, p, eq):
        return jnp.einsum(eq, x, p, preferred_element_type=f32)

    u_real = mm(grad_real, factor_real, "ibr,brc->ibc") + mm(grad_imag, factor_imag, "ibr,brc->ibc")
    u_imag = mm(grad_imag, factor_real, "ibr,brc->ibc") - mm(grad_real, factor_imag, "ibr,brc->ibc")
    back_real = 2.0 * u_real - grad_real.astype(f32)
    back_imag = 2.0 * u_imag - grad_imag.astype(f32)
    back_both = (
        jnp.stack([back_real, back_imag], axis=2)
        .astype(jnp.bfloat16)
        .reshape(image_rows, 2 * bins_local, channels)
    )
    returned = lax.all_to_all(back_both, "freq", split_axis=0, concat_axis=1, tiled=True)
    v_real = mm(input_real, factor_real, "ibk,bck->ibc") - mm(input_imag, factor_imag, "ibk,bck->ibc")
    v_imag = mm(input_real, factor_imag, "ibk,bck->ibc") + mm(input_imag, factor_real, "ibk,bck->ibc")
    local_bins = lax.dynamic_slice_in_dim(
        bin_order, lax.axis_index("freq") * bins_local, bins_local
    )
    cos_local, sin_local = tap_phases(local_bins, GRID)
    cos_t = cos_local.T[:, None, :, None]
    sin_t = sin_local.T[:, None, :, None]
    ur = u_real[None]
    ui = u_imag[None]
    z_t = jnp.stack([cos_t * ur - sin_t * ui, cos_t * ui + sin_t * ur], axis=1).astype(jnp.bfloat16)
    w_t = jnp.stack([cos_t * ur + sin_t * ui, cos_t * ui - sin_t * ur], axis=1).astype(jnp.bfloat16)
    y_all = jnp.stack([v_real, v_imag], axis=0).astype(jnp.bfloat16)
    taps = z_t.shape[0]
    col_share = channels // freq_devices
    row_share = channels // data_devices
    y_cols = y_all.reshape(2, image_rows, bins_local, freq_devices, col_share)
    w_cols = w_t.reshape(taps, 2, image_rows, bins_local, freq_devices, col_share)
    first = jnp.einsum("teibr,eibfc->ftrc", z_t, y_cols, preferred_element_type=f32)
    second = jnp.einsum("eibr,teibfc->ftrc", y_all, w_cols, preferred_element_type=f32)
    gram_scale = 1.0 / math.sqrt(data_devices * freq_devices * slot_count)
    tap_scale = 2.0 * gram_scale / math.sqrt(total_bins)
    col_pieces = ((second - first) * tap_scale).astype(jnp.bfloat16)
    col_pieces = lax.all_to_all(col_pieces, "freq", split_axis=0, concat_axis=0, tiled=True)
    col_sum = jnp.sum(col_pieces.astype(f32), axis=0)
    dp_index = lax.axis_index("dp")
    blocks = col_sum.reshape(taps, data_devices, row_share, col_share)
    step = 1
    while step < data_devices:
        blocks = blocks.reshape(taps, -1, 2, row_share, col_share)
        high = (dp_index // step) % 2 == 1
        keep = jnp.where(high, blocks[:, :, 1], blocks[:, :, 0])
        send = jnp.where(high, blocks[:, :, 0], blocks[:, :, 1])
        pairs = [(i, i ^ step) for i in range(data_devices)]
        blocks = keep + lax.ppermute(send, "dp", pairs)
        step *= 2
    tap_grad = blocks.reshape(taps, row_share, col_share)
    return (returned, tap_grad)


def solution(mesh):
    return jax.shard_map(
        local,
        mesh=mesh,
        in_specs=(
            P(("dp", "freq"), None, None),
            P(("dp", "freq"), None, None),
            P(("dp", "freq")),
            P(),
            P("freq", None, None, None),
        ),
        out_specs=(P(("dp", "freq"), None, None), P(None, "dp", "freq")),
        check_vma=False,
    )
```

```python
import math

import jax
import jax.numpy as jnp
from jax import lax
from jax.sharding import Mesh, PartitionSpec as P

GRID = 32


def dft_table(bin_order, grid_side):
    pixel_index = jnp.arange(grid_side * grid_side, dtype=jnp.int32)
    row_pos = pixel_index // grid_side
    col_pos = pixel_index % grid_side
    freq_u = bin_order // grid_side
    freq_v = bin_order % grid_side
    phase_turns = (
        row_pos[:, None] * freq_u[None, :] + col_pos[:, None] * freq_v[None, :]
    ) % grid_side
    phase_angle = phase_turns.astype(jnp.float32) * (2.0 * math.pi / grid_side)
    both_parts = jnp.stack([jnp.cos(phase_angle), -jnp.sin(phase_angle)], axis=2) / grid_side
    return both_parts.reshape(grid_side * grid_side, -1).astype(jnp.bfloat16)


def tap_phases(bin_order, grid_side):
    offsets = jnp.arange(9, dtype=jnp.int32)
    shift_y = offsets // 3 - 1
    shift_x = offsets % 3 - 1
    freq_u = bin_order // grid_side
    freq_v = bin_order % grid_side
    phase_turns = (
        freq_u[:, None] * shift_y[None, :] + freq_v[:, None] * shift_x[None, :]
    ) % grid_side
    phase_angle = phase_turns.astype(jnp.float32) * (2.0 * math.pi / grid_side)
    return (jnp.cos(phase_angle), jnp.sin(phase_angle))


def local(output_grad, layer_input, counts, bin_order, inverse_factor):
    slot_count, channels, pixels = output_grad.shape
    freq_devices = lax.axis_size("freq")
    data_devices = lax.axis_size("z") * lax.axis_size("c")
    bins_local = inverse_factor.shape[0]
    total_bins = bin_order.shape[0]
    live_mask = (jnp.arange(slot_count, dtype=jnp.int32) < counts[0]).astype(jnp.bfloat16)
    bins_table = dft_table(bin_order, GRID)

    def spectrum(images):
        masked = images * live_mask[:, None, None]
        return jnp.einsum(
            "scp,pk->skc", masked, bins_table, preferred_element_type=jnp.float32
        ).astype(jnp.bfloat16)

    both_spec = jnp.stack([spectrum(output_grad), spectrum(layer_input)], axis=0)
    both_recv = lax.all_to_all(both_spec, "freq", split_axis=2, concat_axis=1, tiled=True)
    image_rows = both_recv.shape[1]
    parts = both_recv.reshape(2, image_rows, bins_local, 2, channels)
    grad_real = parts[0, :, :, 0]
    grad_imag = parts[0, :, :, 1]
    input_real = parts[1, :, :, 0]
    input_imag = parts[1, :, :, 1]
    factor_real = inverse_factor[:, 0]
    factor_imag = inverse_factor[:, 1]
    f32 = jnp.float32

    def mm(x, p, eq):
        return jnp.einsum(eq, x, p, preferred_element_type=f32)

    u_real = mm(grad_real, factor_real, "ibr,brc->ibc") + mm(grad_imag, factor_imag, "ibr,brc->ibc")
    u_imag = mm(grad_imag, factor_real, "ibr,brc->ibc") - mm(grad_real, factor_imag, "ibr,brc->ibc")
    back_real = 2.0 * u_real - grad_real.astype(f32)
    back_imag = 2.0 * u_imag - grad_imag.astype(f32)
    back_both = (
        jnp.stack([back_real, back_imag], axis=2)
        .astype(jnp.bfloat16)
        .reshape(image_rows, 2 * bins_local, channels)
    )
    returned = lax.all_to_all(back_both, "freq", split_axis=0, concat_axis=1, tiled=True)
    v_real = mm(input_real, factor_real, "ibk,bck->ibc") - mm(input_imag, factor_imag, "ibk,bck->ibc")
    v_imag = mm(input_real, factor_imag, "ibk,bck->ibc") + mm(input_imag, factor_real, "ibk,bck->ibc")
    local_bins = lax.dynamic_slice_in_dim(
        bin_order, lax.axis_index("freq") * bins_local, bins_local
    )
    cos_local, sin_local = tap_phases(local_bins, GRID)
    cos_t = cos_local.T[:, None, :, None]
    sin_t = sin_local.T[:, None, :, None]
    ur = u_real[None]
    ui = u_imag[None]
    z_t = jnp.stack([cos_t * ur - sin_t * ui, cos_t * ui + sin_t * ur], axis=1).astype(jnp.bfloat16)
    w_t = jnp.stack([cos_t * ur + sin_t * ui, cos_t * ui - sin_t * ur], axis=1).astype(jnp.bfloat16)
    y_all = jnp.stack([v_real, v_imag], axis=0).astype(jnp.bfloat16)
    taps = z_t.shape[0]
    col_share = channels // freq_devices
    row_share = channels // data_devices
    y_cols = y_all.reshape(2, image_rows, bins_local, freq_devices, col_share)
    w_cols = w_t.reshape(taps, 2, image_rows, bins_local, freq_devices, col_share)
    first = jnp.einsum("teibr,eibfc->ftrc", z_t, y_cols, preferred_element_type=f32)
    second = jnp.einsum("eibr,teibfc->ftrc", y_all, w_cols, preferred_element_type=f32)
    gram_scale = 1.0 / math.sqrt(data_devices * freq_devices * slot_count)
    tap_scale = 2.0 * gram_scale / math.sqrt(total_bins)
    col_pieces = ((second - first) * tap_scale).astype(jnp.bfloat16)
    col_pieces = lax.all_to_all(col_pieces, "freq", split_axis=0, concat_axis=0, tiled=True)
    col_sum = jnp.sum(col_pieces.astype(f32), axis=0)
    z_devices = lax.axis_size("z")
    core_devices = lax.axis_size("c")
    row_pieces = jnp.transpose(
        col_sum.reshape(taps, z_devices, core_devices, row_share, col_share), (2, 1, 0, 3, 4)
    )
    row_pieces = lax.all_to_all(row_pieces, "c", split_axis=0, concat_axis=0, tiled=True)
    row_pieces = jnp.sum(row_pieces, axis=0)
    row_pieces = lax.all_to_all(row_pieces, "z", split_axis=0, concat_axis=0, tiled=True)
    tap_grad = jnp.sum(row_pieces, axis=0)
    return (returned, tap_grad)


def solution(mesh):
    cores = 2
    chips = Mesh(
        mesh.devices.reshape(mesh.shape["dp"] // cores, cores, mesh.shape["freq"]),
        ("z", "c", "freq"),
    )
    return jax.shard_map(
        local,
        mesh=chips,
        in_specs=(
            P(("z", "c", "freq"), None, None),
            P(("z", "c", "freq"), None, None),
            P(("z", "c", "freq")),
            P(),
            P("freq", None, None, None),
        ),
        out_specs=(P(("z", "c", "freq"), None, None), P(None, ("z", "c"), "freq")),
        check_vma=False,
    )
```

```python
import math

import jax
import jax.numpy as jnp
from jax import lax
from jax.sharding import Mesh, PartitionSpec as P

GRID = 32


def dft_table(bin_order, grid_side):
    pixel_index = jnp.arange(grid_side * grid_side, dtype=jnp.int32)
    row_pos = pixel_index // grid_side
    col_pos = pixel_index % grid_side
    freq_u = bin_order // grid_side
    freq_v = bin_order % grid_side
    phase_turns = (
        row_pos[:, None] * freq_u[None, :] + col_pos[:, None] * freq_v[None, :]
    ) % grid_side
    phase_angle = phase_turns.astype(jnp.float32) * (2.0 * math.pi / grid_side)
    both_parts = jnp.stack([jnp.cos(phase_angle), -jnp.sin(phase_angle)], axis=2) / grid_side
    return both_parts.reshape(grid_side * grid_side, -1).astype(jnp.bfloat16)


def tap_phases(bin_order, grid_side):
    offsets = jnp.arange(9, dtype=jnp.int32)
    shift_y = offsets // 3 - 1
    shift_x = offsets % 3 - 1
    freq_u = bin_order // grid_side
    freq_v = bin_order % grid_side
    phase_turns = (
        freq_u[:, None] * shift_y[None, :] + freq_v[:, None] * shift_x[None, :]
    ) % grid_side
    phase_angle = phase_turns.astype(jnp.float32) * (2.0 * math.pi / grid_side)
    return (jnp.cos(phase_angle), jnp.sin(phase_angle))


def local(output_grad, layer_input, counts, bin_order, inverse_factor):
    slot_count, channels, pixels = output_grad.shape
    freq_devices = lax.axis_size("freq")
    data_devices = lax.axis_size("z") * lax.axis_size("c")
    bins_local = inverse_factor.shape[0]
    total_bins = bin_order.shape[0]
    live_mask = (jnp.arange(slot_count, dtype=jnp.int32) < counts[0]).astype(jnp.bfloat16)
    bins_table = dft_table(bin_order, GRID)

    def spectrum(images):
        masked = images * live_mask[:, None, None]
        return jnp.einsum(
            "scp,pk->skc", masked, bins_table, preferred_element_type=jnp.float32
        ).astype(jnp.bfloat16)

    both_spec = jnp.stack([spectrum(output_grad), spectrum(layer_input)], axis=0)
    both_recv = lax.all_to_all(both_spec, "freq", split_axis=2, concat_axis=1, tiled=True)
    image_rows = both_recv.shape[1]
    parts = both_recv.reshape(2, image_rows, bins_local, 2, channels)
    grad_real = parts[0, :, :, 0]
    grad_imag = parts[0, :, :, 1]
    input_real = parts[1, :, :, 0]
    input_imag = parts[1, :, :, 1]
    f32 = jnp.float32

    u_lhs = jnp.stack(
        [jnp.stack([grad_real, grad_imag], axis=2), jnp.stack([grad_imag, -grad_real], axis=2)]
    )
    v_lhs = jnp.stack(
        [jnp.stack([input_real, -input_imag], axis=2), jnp.stack([input_imag, input_real], axis=2)]
    )
    u_both = jnp.einsum("eibpr,bprc->eibc", u_lhs, inverse_factor, preferred_element_type=f32)
    v_both = jnp.einsum("eibpk,bpck->eibc", v_lhs, inverse_factor, preferred_element_type=f32)
    u_real = u_both[0]
    u_imag = u_both[1]
    back_real = 2.0 * u_real - grad_real.astype(f32)
    back_imag = 2.0 * u_imag - grad_imag.astype(f32)
    back_both = (
        jnp.stack([back_real, back_imag], axis=2)
        .astype(jnp.bfloat16)
        .reshape(image_rows, 2 * bins_local, channels)
    )
    returned = lax.all_to_all(back_both, "freq", split_axis=0, concat_axis=1, tiled=True)
    local_bins = lax.dynamic_slice_in_dim(
        bin_order, lax.axis_index("freq") * bins_local, bins_local
    )
    cos_local, sin_local = tap_phases(local_bins, GRID)
    cos_t = cos_local.T[:, None, :, None]
    sin_t = sin_local.T[:, None, :, None]
    ur = u_real[None]
    ui = u_imag[None]
    z_t = jnp.stack([cos_t * ur - sin_t * ui, cos_t * ui + sin_t * ur], axis=1).astype(jnp.bfloat16)
    w_t = jnp.stack([cos_t * ur + sin_t * ui, cos_t * ui - sin_t * ur], axis=1).astype(jnp.bfloat16)
    y_all = v_both.astype(jnp.bfloat16)
    taps = z_t.shape[0]
    col_share = channels // freq_devices
    row_share = channels // data_devices
    y_cols = y_all.reshape(2, image_rows, bins_local, freq_devices, col_share)
    w_cols = w_t.reshape(taps, 2, image_rows, bins_local, freq_devices, col_share)
    first = jnp.einsum("teibr,eibfc->ftrc", z_t, y_cols, preferred_element_type=f32)
    second = jnp.einsum("eibr,teibfc->ftrc", y_all, w_cols, preferred_element_type=f32)
    gram_scale = 1.0 / math.sqrt(data_devices * freq_devices * slot_count)
    tap_scale = 2.0 * gram_scale / math.sqrt(total_bins)
    col_pieces = ((second - first) * tap_scale).astype(jnp.bfloat16)
    col_pieces = lax.all_to_all(col_pieces, "freq", split_axis=0, concat_axis=0, tiled=True)
    z_devices = lax.axis_size("z")
    core_devices = lax.axis_size("c")
    block = taps * row_share * col_share
    col_sum = jnp.sum(
        col_pieces.reshape(
            freq_devices, taps, z_devices, core_devices, row_share, col_share
        ).astype(f32),
        axis=0,
    )
    row_pieces = jnp.transpose(col_sum, (2, 1, 0, 3, 4)).reshape(core_devices, z_devices * block)
    row_pieces = lax.all_to_all(row_pieces, "c", split_axis=0, concat_axis=0, tiled=True)
    row_pieces = jnp.sum(row_pieces, axis=0).reshape(z_devices, block)
    row_pieces = lax.all_to_all(row_pieces, "z", split_axis=0, concat_axis=0, tiled=True)
    tap_grad = jnp.sum(row_pieces, axis=0).reshape(taps, row_share, col_share)
    return (returned, tap_grad)


def solution(mesh):
    cores = 2
    chips = Mesh(
        mesh.devices.reshape(mesh.shape["dp"] // cores, cores, mesh.shape["freq"]),
        ("z", "c", "freq"),
    )
    return jax.shard_map(
        local,
        mesh=chips,
        in_specs=(
            P(("z", "c", "freq"), None, None),
            P(("z", "c", "freq"), None, None),
            P(("z", "c", "freq")),
            P(),
            P("freq", None, None, None),
        ),
        out_specs=(P(("z", "c", "freq"), None, None), P(None, ("z", "c"), "freq")),
        check_vma=False,
    )
```

```python
import math

import jax
import jax.numpy as jnp
from jax import lax
from jax.sharding import Mesh, PartitionSpec as P

GRID = 32


def dft_table(bin_order, grid_side):
    pixel_index = jnp.arange(grid_side * grid_side, dtype=jnp.int32)
    row_pos = pixel_index // grid_side
    col_pos = pixel_index % grid_side
    freq_u = bin_order // grid_side
    freq_v = bin_order % grid_side
    phase_turns = (
        row_pos[:, None] * freq_u[None, :] + col_pos[:, None] * freq_v[None, :]
    ) % grid_side
    phase_angle = phase_turns.astype(jnp.float32) * (2.0 * math.pi / grid_side)
    both_parts = jnp.stack([jnp.cos(phase_angle), -jnp.sin(phase_angle)], axis=2) / grid_side
    return both_parts.reshape(grid_side * grid_side, -1).astype(jnp.bfloat16)


def tap_phases(bin_order, grid_side):
    offsets = jnp.arange(9, dtype=jnp.int32)
    shift_y = offsets // 3 - 1
    shift_x = offsets % 3 - 1
    freq_u = bin_order // grid_side
    freq_v = bin_order % grid_side
    phase_turns = (
        freq_u[:, None] * shift_y[None, :] + freq_v[:, None] * shift_x[None, :]
    ) % grid_side
    phase_angle = phase_turns.astype(jnp.float32) * (2.0 * math.pi / grid_side)
    return (jnp.cos(phase_angle), jnp.sin(phase_angle))


def local(output_grad, layer_input, counts, bin_order, inverse_factor):
    slot_count, channels, pixels = output_grad.shape
    freq_devices = lax.axis_size("freq")
    data_devices = lax.axis_size("z") * lax.axis_size("c")
    bins_local = inverse_factor.shape[0]
    total_bins = bin_order.shape[0]
    live_mask = (jnp.arange(slot_count, dtype=jnp.int32) < counts[0]).astype(jnp.bfloat16)
    bins_table = dft_table(bin_order, GRID)

    def spectrum(images):
        masked = images * live_mask[:, None, None]
        return jnp.einsum(
            "scp,pk->skc", masked, bins_table, preferred_element_type=jnp.float32
        ).astype(jnp.bfloat16)

    both_spec = jnp.stack([spectrum(output_grad), spectrum(layer_input)], axis=0)
    both_recv = lax.all_to_all(both_spec, "freq", split_axis=2, concat_axis=1, tiled=True)
    image_rows = both_recv.shape[1]
    parts = both_recv.reshape(2, image_rows, bins_local, 2, channels)
    grad_real = parts[0, :, :, 0]
    grad_imag = parts[0, :, :, 1]
    input_real = parts[1, :, :, 0]
    input_imag = parts[1, :, :, 1]
    factor_real = inverse_factor[:, 0]
    factor_imag = inverse_factor[:, 1]
    f32 = jnp.float32

    def mm(x, p, eq):
        return jnp.einsum(eq, x, p, preferred_element_type=f32)

    u_real = mm(grad_real, factor_real, "ibr,brc->ibc") + mm(grad_imag, factor_imag, "ibr,brc->ibc")
    u_imag = mm(grad_imag, factor_real, "ibr,brc->ibc") - mm(grad_real, factor_imag, "ibr,brc->ibc")
    back_real = 2.0 * u_real - grad_real.astype(f32)
    back_imag = 2.0 * u_imag - grad_imag.astype(f32)
    back_both = (
        jnp.stack([back_real, back_imag], axis=2)
        .astype(jnp.bfloat16)
        .reshape(image_rows, 2 * bins_local, channels)
    )
    returned = lax.all_to_all(back_both, "freq", split_axis=0, concat_axis=1, tiled=True)
    v_real = mm(input_real, factor_real, "ibk,bck->ibc") - mm(input_imag, factor_imag, "ibk,bck->ibc")
    v_imag = mm(input_real, factor_imag, "ibk,bck->ibc") + mm(input_imag, factor_real, "ibk,bck->ibc")
    local_bins = lax.dynamic_slice_in_dim(
        bin_order, lax.axis_index("freq") * bins_local, bins_local
    )
    cos_local, sin_local = tap_phases(local_bins, GRID)
    cos_t = cos_local.T[:, None, :, None]
    sin_t = sin_local.T[:, None, :, None]
    ur = u_real[None]
    ui = u_imag[None]
    z_t = jnp.stack([cos_t * ur - sin_t * ui, cos_t * ui + sin_t * ur], axis=1).astype(jnp.bfloat16)
    w_t = jnp.stack([cos_t * ur + sin_t * ui, cos_t * ui - sin_t * ur], axis=1).astype(jnp.bfloat16)
    y_all = jnp.stack([v_real, v_imag], axis=0).astype(jnp.bfloat16)
    returned, z_t, w_t, y_all = lax.optimization_barrier((returned, z_t, w_t, y_all))
    taps = z_t.shape[0]
    col_share = channels // freq_devices
    row_share = channels // data_devices
    y_cols = y_all.reshape(2, image_rows, bins_local, freq_devices, col_share)
    w_cols = w_t.reshape(taps, 2, image_rows, bins_local, freq_devices, col_share)
    first = jnp.einsum("teibr,eibfc->ftrc", z_t, y_cols, preferred_element_type=f32)
    second = jnp.einsum("eibr,teibfc->ftrc", y_all, w_cols, preferred_element_type=f32)
    gram_scale = 1.0 / math.sqrt(data_devices * freq_devices * slot_count)
    tap_scale = 2.0 * gram_scale / math.sqrt(total_bins)
    col_pieces = ((second - first) * tap_scale).astype(jnp.bfloat16)
    col_pieces = lax.all_to_all(col_pieces, "freq", split_axis=0, concat_axis=0, tiled=True)
    col_sum = jnp.sum(col_pieces.astype(f32), axis=0)
    z_devices = lax.axis_size("z")
    core_devices = lax.axis_size("c")
    row_pieces = jnp.transpose(
        col_sum.reshape(taps, z_devices, core_devices, row_share, col_share), (2, 1, 0, 3, 4)
    )
    row_pieces = lax.all_to_all(row_pieces, "c", split_axis=0, concat_axis=0, tiled=True)
    row_pieces = jnp.sum(row_pieces, axis=0).astype(jnp.bfloat16)
    row_pieces = lax.all_to_all(row_pieces, "z", split_axis=0, concat_axis=0, tiled=True)
    tap_grad = jnp.sum(row_pieces.astype(f32), axis=0)
    return (returned, tap_grad)


def solution(mesh):
    cores = 2
    chips = Mesh(
        mesh.devices.reshape(mesh.shape["dp"] // cores, cores, mesh.shape["freq"]),
        ("z", "c", "freq"),
    )
    return jax.shard_map(
        local,
        mesh=chips,
        in_specs=(
            P(("z", "c", "freq"), None, None),
            P(("z", "c", "freq"), None, None),
            P(("z", "c", "freq")),
            P(),
            P("freq", None, None, None),
        ),
        out_specs=(P(("z", "c", "freq"), None, None), P(None, ("z", "c"), "freq")),
        check_vma=False,
    )
```

```python
import math

import jax
import jax.numpy as jnp
from jax import lax
from jax.sharding import Mesh, PartitionSpec as P

GRID = 32


def dft_table(bin_order, grid_side):
    pixel_index = jnp.arange(grid_side * grid_side, dtype=jnp.int32)
    row_pos = pixel_index // grid_side
    col_pos = pixel_index % grid_side
    freq_u = bin_order // grid_side
    freq_v = bin_order % grid_side
    phase_turns = (
        row_pos[:, None] * freq_u[None, :] + col_pos[:, None] * freq_v[None, :]
    ) % grid_side
    phase_angle = phase_turns.astype(jnp.float32) * (2.0 * math.pi / grid_side)
    both_parts = jnp.stack([jnp.cos(phase_angle), -jnp.sin(phase_angle)], axis=2) / grid_side
    return both_parts.reshape(grid_side * grid_side, -1).astype(jnp.bfloat16)


def tap_phases(bin_order, grid_side):
    offsets = jnp.arange(9, dtype=jnp.int32)
    shift_y = offsets // 3 - 1
    shift_x = offsets % 3 - 1
    freq_u = bin_order // grid_side
    freq_v = bin_order % grid_side
    phase_turns = (
        freq_u[:, None] * shift_y[None, :] + freq_v[:, None] * shift_x[None, :]
    ) % grid_side
    phase_angle = phase_turns.astype(jnp.float32) * (2.0 * math.pi / grid_side)
    return (jnp.cos(phase_angle), jnp.sin(phase_angle))


def local(output_grad, layer_input, counts, bin_order, inverse_factor):
    slot_count, channels, pixels = output_grad.shape
    freq_devices = lax.axis_size("freq")
    data_devices = lax.axis_size("z") * lax.axis_size("c")
    bins_local = inverse_factor.shape[0]
    total_bins = bin_order.shape[0]
    live_mask = (jnp.arange(slot_count, dtype=jnp.int32) < counts[0]).astype(jnp.bfloat16)
    bins_table = dft_table(bin_order, GRID)

    def spectrum(images):
        masked = images * live_mask[:, None, None]
        return jnp.einsum(
            "scp,pk->skc", masked, bins_table, preferred_element_type=jnp.float32
        ).astype(jnp.bfloat16)

    both_spec = jnp.stack([spectrum(output_grad), spectrum(layer_input)], axis=0)
    both_recv = lax.all_to_all(both_spec, "freq", split_axis=2, concat_axis=1, tiled=True)
    image_rows = both_recv.shape[1]
    parts = both_recv.reshape(2, image_rows, bins_local, 2, channels)
    grad_real = parts[0, :, :, 0]
    grad_imag = parts[0, :, :, 1]
    input_real = parts[1, :, :, 0]
    input_imag = parts[1, :, :, 1]
    factor_real = inverse_factor[:, 0]
    factor_imag = inverse_factor[:, 1]
    f32 = jnp.float32

    def mm(x, p, eq):
        return jnp.einsum(eq, x, p, preferred_element_type=f32)

    u_real = mm(grad_real, factor_real, "ibr,brc->ibc") + mm(grad_imag, factor_imag, "ibr,brc->ibc")
    u_imag = mm(grad_imag, factor_real, "ibr,brc->ibc") - mm(grad_real, factor_imag, "ibr,brc->ibc")
    back_real = 2.0 * u_real - grad_real.astype(f32)
    back_imag = 2.0 * u_imag - grad_imag.astype(f32)
    back_both = (
        jnp.stack([back_real, back_imag], axis=2)
        .astype(jnp.bfloat16)
        .reshape(image_rows, 2 * bins_local, channels)
    )
    returned = lax.all_to_all(back_both, "freq", split_axis=0, concat_axis=1, tiled=True)
    v_real = mm(input_real, factor_real, "ibk,bck->ibc") - mm(input_imag, factor_imag, "ibk,bck->ibc")
    v_imag = mm(input_real, factor_imag, "ibk,bck->ibc") + mm(input_imag, factor_real, "ibk,bck->ibc")
    local_bins = lax.dynamic_slice_in_dim(
        bin_order, lax.axis_index("freq") * bins_local, bins_local
    )
    cos_local, sin_local = tap_phases(local_bins, GRID)
    returned, cos_local, sin_local = lax.optimization_barrier((returned, cos_local, sin_local))
    cos_t = cos_local.T[:, None, :, None]
    sin_t = sin_local.T[:, None, :, None]
    ur = u_real[None]
    ui = u_imag[None]
    z_t = jnp.stack([cos_t * ur - sin_t * ui, cos_t * ui + sin_t * ur], axis=1).astype(jnp.bfloat16)
    w_t = jnp.stack([cos_t * ur + sin_t * ui, cos_t * ui - sin_t * ur], axis=1).astype(jnp.bfloat16)
    y_all = jnp.stack([v_real, v_imag], axis=0).astype(jnp.bfloat16)
    taps = z_t.shape[0]
    col_share = channels // freq_devices
    row_share = channels // data_devices
    y_cols = y_all.reshape(2, image_rows, bins_local, freq_devices, col_share)
    w_cols = w_t.reshape(taps, 2, image_rows, bins_local, freq_devices, col_share)
    first = jnp.einsum("teibr,eibfc->ftrc", z_t, y_cols, preferred_element_type=f32)
    second = jnp.einsum("eibr,teibfc->ftrc", y_all, w_cols, preferred_element_type=f32)
    gram_scale = 1.0 / math.sqrt(data_devices * freq_devices * slot_count)
    tap_scale = 2.0 * gram_scale / math.sqrt(total_bins)
    col_pieces = ((second - first) * tap_scale).astype(jnp.bfloat16)
    col_pieces = lax.all_to_all(col_pieces, "freq", split_axis=0, concat_axis=0, tiled=True)
    col_sum = jnp.sum(col_pieces.astype(f32), axis=0)
    z_devices = lax.axis_size("z")
    core_devices = lax.axis_size("c")
    row_pieces = jnp.transpose(
        col_sum.reshape(taps, z_devices, core_devices, row_share, col_share), (2, 1, 0, 3, 4)
    )
    row_pieces = lax.all_to_all(row_pieces, "c", split_axis=0, concat_axis=0, tiled=True)
    row_pieces = jnp.sum(row_pieces, axis=0)
    row_pieces = lax.all_to_all(row_pieces, "z", split_axis=0, concat_axis=0, tiled=True)
    tap_grad = jnp.sum(row_pieces, axis=0)
    return (returned, tap_grad)


def solution(mesh):
    cores = 2
    chips = Mesh(
        mesh.devices.reshape(mesh.shape["dp"] // cores, cores, mesh.shape["freq"]),
        ("z", "c", "freq"),
    )
    return jax.shard_map(
        local,
        mesh=chips,
        in_specs=(
            P(("z", "c", "freq"), None, None),
            P(("z", "c", "freq"), None, None),
            P(("z", "c", "freq")),
            P(),
            P("freq", None, None, None),
        ),
        out_specs=(P(("z", "c", "freq"), None, None), P(None, ("z", "c"), "freq")),
        check_vma=False,
    )
```

```python
import math

import jax
import jax.numpy as jnp
from jax import lax
from jax.sharding import Mesh, PartitionSpec as P

GRID = 32


def dft_table(bin_order, grid_side):
    pixel_index = jnp.arange(grid_side * grid_side, dtype=jnp.int32)
    row_pos = pixel_index // grid_side
    col_pos = pixel_index % grid_side
    freq_u = bin_order // grid_side
    freq_v = bin_order % grid_side
    phase_turns = (
        row_pos[:, None] * freq_u[None, :] + col_pos[:, None] * freq_v[None, :]
    ) % grid_side
    phase_angle = phase_turns.astype(jnp.float32) * (2.0 * math.pi / grid_side)
    both_parts = jnp.stack([jnp.cos(phase_angle), -jnp.sin(phase_angle)], axis=2) / grid_side
    return both_parts.reshape(grid_side * grid_side, -1).astype(jnp.bfloat16)


def tap_phases(bin_order, grid_side):
    offsets = jnp.arange(9, dtype=jnp.int32)
    shift_y = offsets // 3 - 1
    shift_x = offsets % 3 - 1
    freq_u = bin_order // grid_side
    freq_v = bin_order % grid_side
    phase_turns = (
        freq_u[:, None] * shift_y[None, :] + freq_v[:, None] * shift_x[None, :]
    ) % grid_side
    phase_angle = phase_turns.astype(jnp.float32) * (2.0 * math.pi / grid_side)
    return (jnp.cos(phase_angle), jnp.sin(phase_angle))


def local(output_grad, layer_input, counts, bin_order, inverse_factor):
    slot_count, channels, pixels = output_grad.shape
    freq_devices = lax.axis_size("freq")
    data_devices = lax.axis_size("z") * lax.axis_size("c")
    bins_local = inverse_factor.shape[0]
    total_bins = bin_order.shape[0]
    live_mask = (jnp.arange(slot_count, dtype=jnp.int32) < counts[0]).astype(jnp.bfloat16)
    bins_table = dft_table(bin_order, GRID)

    def spectrum(images):
        masked = images * live_mask[:, None, None]
        return jnp.einsum(
            "scp,pk->skc", masked, bins_table, preferred_element_type=jnp.float32
        ).astype(jnp.bfloat16)

    both_spec = jnp.stack([spectrum(output_grad), spectrum(layer_input)], axis=0)
    both_recv = lax.all_to_all(both_spec, "freq", split_axis=2, concat_axis=1, tiled=True)
    image_rows = both_recv.shape[1]
    parts = both_recv.reshape(2, image_rows, bins_local, 2, channels)
    grad_real = parts[0, :, :, 0]
    grad_imag = parts[0, :, :, 1]
    input_real = parts[1, :, :, 0]
    input_imag = parts[1, :, :, 1]
    factor_real = inverse_factor[:, 0]
    factor_imag = inverse_factor[:, 1]
    f32 = jnp.float32

    def mm(x, p, eq):
        return jnp.einsum(eq, x, p, preferred_element_type=f32)

    u_real = mm(grad_real, factor_real, "ibr,brc->ibc") + mm(grad_imag, factor_imag, "ibr,brc->ibc")
    u_imag = mm(grad_imag, factor_real, "ibr,brc->ibc") - mm(grad_real, factor_imag, "ibr,brc->ibc")
    back_real = 2.0 * u_real - grad_real.astype(f32)
    back_imag = 2.0 * u_imag - grad_imag.astype(f32)
    back_both = (
        jnp.stack([back_real, back_imag], axis=2)
        .astype(jnp.bfloat16)
        .reshape(image_rows, 2 * bins_local, channels)
    )
    returned = lax.all_to_all(back_both, "freq", split_axis=0, concat_axis=1, tiled=True)
    v_real = mm(input_real, factor_real, "ibk,bck->ibc") - mm(input_imag, factor_imag, "ibk,bck->ibc")
    v_imag = mm(input_real, factor_imag, "ibk,bck->ibc") + mm(input_imag, factor_real, "ibk,bck->ibc")
    local_bins = lax.dynamic_slice_in_dim(
        bin_order, lax.axis_index("freq") * bins_local, bins_local
    )
    cos_local, sin_local = tap_phases(local_bins, GRID)
    cos_t = cos_local.T[:, None, :, None]
    sin_t = sin_local.T[:, None, :, None]
    ur = u_real[None]
    ui = u_imag[None]
    z_t = jnp.stack([cos_t * ur - sin_t * ui, cos_t * ui + sin_t * ur], axis=1).astype(jnp.bfloat16)
    w_t = jnp.stack([cos_t * ur + sin_t * ui, cos_t * ui - sin_t * ur], axis=1).astype(jnp.bfloat16)
    y_all = jnp.stack([v_real, v_imag], axis=0).astype(jnp.bfloat16)
    taps = z_t.shape[0]
    col_share = channels // freq_devices
    row_share = channels // data_devices
    y_cols = y_all.reshape(2, image_rows, bins_local, freq_devices, col_share)
    w_cols = w_t.reshape(taps, 2, image_rows, bins_local, freq_devices, col_share)
    first = jnp.einsum("teibr,eibfc->ftrc", z_t, y_cols, preferred_element_type=f32)
    second = jnp.einsum("eibr,teibfc->ftrc", y_all, w_cols, preferred_element_type=f32)
    gram_scale = 1.0 / math.sqrt(data_devices * freq_devices * slot_count)
    tap_scale = 2.0 * gram_scale / math.sqrt(total_bins)
    z_devices = lax.axis_size("z")
    core_devices = lax.axis_size("c")
    block = taps * row_share * col_share
    col_pieces = ((second - first) * tap_scale).reshape(
        freq_devices, taps, z_devices, core_devices, row_share, col_share
    )
    col_pieces = jnp.transpose(col_pieces, (0, 3, 2, 1, 4, 5)).reshape(
        freq_devices, core_devices * z_devices * block
    ).astype(jnp.bfloat16)
    col_pieces = lax.all_to_all(col_pieces, "freq", split_axis=0, concat_axis=0, tiled=True)
    row_pieces = jnp.sum(col_pieces.astype(f32), axis=0).reshape(core_devices, z_devices * block)
    row_pieces = lax.all_to_all(row_pieces, "c", split_axis=0, concat_axis=0, tiled=True)
    row_pieces = jnp.sum(row_pieces, axis=0).reshape(z_devices, block)
    row_pieces = lax.all_to_all(row_pieces, "z", split_axis=0, concat_axis=0, tiled=True)
    tap_grad = jnp.sum(row_pieces, axis=0).reshape(taps, row_share, col_share)
    return (returned, tap_grad)


def solution(mesh):
    cores = 2
    chips = Mesh(
        mesh.devices.reshape(mesh.shape["dp"] // cores, cores, mesh.shape["freq"]),
        ("z", "c", "freq"),
    )
    return jax.shard_map(
        local,
        mesh=chips,
        in_specs=(
            P(("z", "c", "freq"), None, None),
            P(("z", "c", "freq"), None, None),
            P(("z", "c", "freq")),
            P(),
            P("freq", None, None, None),
        ),
        out_specs=(P(("z", "c", "freq"), None, None), P(None, ("z", "c"), "freq")),
        check_vma=False,
    )
```

```python
import math

import jax
import jax.numpy as jnp
from jax import lax
from jax.sharding import Mesh, PartitionSpec as P

GRID = 32


def dft_table(bin_order, grid_side):
    pixel_index = jnp.arange(grid_side * grid_side, dtype=jnp.int32)
    row_pos = pixel_index // grid_side
    col_pos = pixel_index % grid_side
    freq_u = bin_order // grid_side
    freq_v = bin_order % grid_side
    phase_turns = (
        row_pos[:, None] * freq_u[None, :] + col_pos[:, None] * freq_v[None, :]
    ) % grid_side
    phase_angle = phase_turns.astype(jnp.float32) * (2.0 * math.pi / grid_side)
    both_parts = jnp.stack([jnp.cos(phase_angle), -jnp.sin(phase_angle)], axis=2) / grid_side
    return both_parts.reshape(grid_side * grid_side, -1).astype(jnp.bfloat16)


def tap_phases(bin_order, grid_side):
    offsets = jnp.arange(9, dtype=jnp.int32)
    shift_y = offsets // 3 - 1
    shift_x = offsets % 3 - 1
    freq_u = bin_order // grid_side
    freq_v = bin_order % grid_side
    phase_turns = (
        freq_u[:, None] * shift_y[None, :] + freq_v[:, None] * shift_x[None, :]
    ) % grid_side
    phase_angle = phase_turns.astype(jnp.float32) * (2.0 * math.pi / grid_side)
    return (jnp.cos(phase_angle), jnp.sin(phase_angle))


def local(output_grad, layer_input, counts, bin_order, inverse_factor):
    slot_count, channels, pixels = output_grad.shape
    freq_devices = lax.axis_size("freq")
    data_devices = lax.axis_size("z") * lax.axis_size("c")
    bins_local = inverse_factor.shape[0]
    total_bins = bin_order.shape[0]
    live_mask = (jnp.arange(slot_count, dtype=jnp.int32) < counts[0]).astype(jnp.bfloat16)
    bins_table = dft_table(bin_order, GRID)

    def spectrum(images):
        masked = images * live_mask[:, None, None]
        return jnp.einsum(
            "scp,pk->skc", masked, bins_table, preferred_element_type=jnp.float32
        ).astype(jnp.bfloat16)

    both_spec = jnp.stack([spectrum(output_grad), spectrum(layer_input)], axis=0)
    both_recv = lax.all_to_all(both_spec, "freq", split_axis=2, concat_axis=1, tiled=True)
    image_rows = both_recv.shape[1]
    parts = both_recv.reshape(2, image_rows, bins_local, 2, channels)
    grad_real = parts[0, :, :, 0]
    grad_imag = parts[0, :, :, 1]
    input_real = parts[1, :, :, 0]
    input_imag = parts[1, :, :, 1]
    factor_real = inverse_factor[:, 0]
    factor_imag = inverse_factor[:, 1]
    f32 = jnp.float32

    def mm(x, p, eq):
        return jnp.einsum(eq, x, p, preferred_element_type=f32)

    u_real = mm(grad_real, factor_real, "ibr,brc->ibc") + mm(grad_imag, factor_imag, "ibr,brc->ibc")
    u_imag = mm(grad_imag, factor_real, "ibr,brc->ibc") - mm(grad_real, factor_imag, "ibr,brc->ibc")
    back_real = 2.0 * u_real - grad_real.astype(f32)
    back_imag = 2.0 * u_imag - grad_imag.astype(f32)
    back_both = (
        jnp.stack([back_real, back_imag], axis=2)
        .astype(jnp.bfloat16)
        .reshape(image_rows, 2 * bins_local, channels)
    )
    returned = lax.all_to_all(back_both, "freq", split_axis=0, concat_axis=1, tiled=True)
    v_real = mm(input_real, factor_real, "ibk,bck->ibc") - mm(input_imag, factor_imag, "ibk,bck->ibc")
    v_imag = mm(input_real, factor_imag, "ibk,bck->ibc") + mm(input_imag, factor_real, "ibk,bck->ibc")
    local_bins = lax.dynamic_slice_in_dim(
        bin_order, lax.axis_index("freq") * bins_local, bins_local
    )
    cos_local, sin_local = tap_phases(local_bins, GRID)
    cos_t = cos_local.T[:, None, :, None]
    sin_t = sin_local.T[:, None, :, None]
    ur = u_real[None]
    ui = u_imag[None]
    z_t = jnp.stack([cos_t * ur - sin_t * ui, cos_t * ui + sin_t * ur], axis=1).astype(jnp.bfloat16)
    w_t = jnp.stack([cos_t * ur + sin_t * ui, cos_t * ui - sin_t * ur], axis=1).astype(jnp.bfloat16)
    y_all = jnp.stack([v_real, v_imag], axis=0).astype(jnp.bfloat16)
    taps = z_t.shape[0]
    col_share = channels // freq_devices
    row_share = channels // data_devices
    y_cols = y_all.reshape(2, image_rows, bins_local, freq_devices, col_share)
    w_cols = w_t.reshape(taps, 2, image_rows, bins_local, freq_devices, col_share)
    first = jnp.einsum("teibr,eibfc->ftrc", z_t, y_cols, preferred_element_type=f32)
    second = jnp.einsum("eibr,teibfc->ftrc", y_all, w_cols, preferred_element_type=f32)
    gram_scale = 1.0 / math.sqrt(data_devices * freq_devices * slot_count)
    tap_scale = 2.0 * gram_scale / math.sqrt(total_bins)
    col_pieces = ((second - first) * tap_scale).astype(jnp.bfloat16)
    col_pieces = lax.all_to_all(col_pieces, "freq", split_axis=0, concat_axis=0, tiled=True)
    col_sum = jnp.sum(col_pieces.astype(f32), axis=0)
    z_devices = lax.axis_size("z")
    core_devices = lax.axis_size("c")
    row_pieces = jnp.transpose(
        col_sum.astype(jnp.bfloat16).reshape(taps, z_devices, core_devices, row_share, col_share),
        (2, 1, 0, 3, 4),
    )
    row_pieces = lax.all_to_all(row_pieces, "c", split_axis=0, concat_axis=0, tiled=True)
    row_pieces = jnp.sum(row_pieces.astype(f32), axis=0).astype(jnp.bfloat16)
    row_pieces = lax.all_to_all(row_pieces, "z", split_axis=0, concat_axis=0, tiled=True)
    tap_grad = jnp.sum(row_pieces.astype(f32), axis=0)
    return (returned, tap_grad)


def solution(mesh):
    cores = 2
    chips = Mesh(
        mesh.devices.reshape(mesh.shape["dp"] // cores, cores, mesh.shape["freq"]),
        ("z", "c", "freq"),
    )
    return jax.shard_map(
        local,
        mesh=chips,
        in_specs=(
            P(("z", "c", "freq"), None, None),
            P(("z", "c", "freq"), None, None),
            P(("z", "c", "freq")),
            P(),
            P("freq", None, None, None),
        ),
        out_specs=(P(("z", "c", "freq"), None, None), P(None, ("z", "c"), "freq")),
        check_vma=False,
    )
```

```python
import math

import jax
import jax.numpy as jnp
from jax import lax
from jax.sharding import Mesh, PartitionSpec as P

GRID = 32


def dft_table(bin_order, grid_side):
    pixel_index = jnp.arange(grid_side * grid_side, dtype=jnp.int32)
    row_pos = pixel_index // grid_side
    col_pos = pixel_index % grid_side
    freq_u = bin_order // grid_side
    freq_v = bin_order % grid_side
    phase_turns = (
        row_pos[:, None] * freq_u[None, :] + col_pos[:, None] * freq_v[None, :]
    ) % grid_side
    phase_angle = phase_turns.astype(jnp.float32) * (2.0 * math.pi / grid_side)
    both_parts = jnp.stack([jnp.cos(phase_angle), -jnp.sin(phase_angle)], axis=2) / grid_side
    return both_parts.reshape(grid_side * grid_side, -1).astype(jnp.bfloat16)


def tap_phases(bin_order, grid_side):
    offsets = jnp.arange(9, dtype=jnp.int32)
    shift_y = offsets // 3 - 1
    shift_x = offsets % 3 - 1
    freq_u = bin_order // grid_side
    freq_v = bin_order % grid_side
    phase_turns = (
        freq_u[:, None] * shift_y[None, :] + freq_v[:, None] * shift_x[None, :]
    ) % grid_side
    phase_angle = phase_turns.astype(jnp.float32) * (2.0 * math.pi / grid_side)
    return (jnp.cos(phase_angle), jnp.sin(phase_angle))


def local(output_grad, layer_input, counts, bin_order, inverse_factor):
    slot_count, channels, pixels = output_grad.shape
    freq_devices = lax.axis_size("freq")
    data_devices = lax.axis_size("z") * lax.axis_size("c")
    bins_local = inverse_factor.shape[0]
    total_bins = bin_order.shape[0]
    live_mask = (jnp.arange(slot_count, dtype=jnp.int32) < counts[0]).astype(jnp.bfloat16)
    bins_table = dft_table(bin_order, GRID)

    def spectrum(images):
        full = jnp.einsum("scp,pk->skc", images, bins_table, preferred_element_type=jnp.float32)
        return (full * live_mask.astype(jnp.float32)[:, None, None]).astype(jnp.bfloat16)

    both_spec = jnp.stack([spectrum(output_grad), spectrum(layer_input)], axis=0)
    both_recv = lax.all_to_all(both_spec, "freq", split_axis=2, concat_axis=1, tiled=True)
    image_rows = both_recv.shape[1]
    parts = both_recv.reshape(2, image_rows, bins_local, 2, channels)
    grad_real = parts[0, :, :, 0]
    grad_imag = parts[0, :, :, 1]
    input_real = parts[1, :, :, 0]
    input_imag = parts[1, :, :, 1]
    factor_real = inverse_factor[:, 0]
    factor_imag = inverse_factor[:, 1]
    f32 = jnp.float32

    def mm(x, p, eq):
        return jnp.einsum(eq, x, p, preferred_element_type=f32)

    u_real = mm(grad_real, factor_real, "ibr,brc->ibc") + mm(grad_imag, factor_imag, "ibr,brc->ibc")
    u_imag = mm(grad_imag, factor_real, "ibr,brc->ibc") - mm(grad_real, factor_imag, "ibr,brc->ibc")
    back_real = 2.0 * u_real - grad_real.astype(f32)
    back_imag = 2.0 * u_imag - grad_imag.astype(f32)
    back_both = (
        jnp.stack([back_real, back_imag], axis=2)
        .astype(jnp.bfloat16)
        .reshape(image_rows, 2 * bins_local, channels)
    )
    returned = lax.all_to_all(back_both, "freq", split_axis=0, concat_axis=1, tiled=True)
    v_real = mm(input_real, factor_real, "ibk,bck->ibc") - mm(input_imag, factor_imag, "ibk,bck->ibc")
    v_imag = mm(input_real, factor_imag, "ibk,bck->ibc") + mm(input_imag, factor_real, "ibk,bck->ibc")
    local_bins = lax.dynamic_slice_in_dim(
        bin_order, lax.axis_index("freq") * bins_local, bins_local
    )
    cos_local, sin_local = tap_phases(local_bins, GRID)
    cos_t = cos_local.T[:, None, :, None]
    sin_t = sin_local.T[:, None, :, None]
    ur = u_real[None]
    ui = u_imag[None]
    z_t = jnp.stack([cos_t * ur - sin_t * ui, cos_t * ui + sin_t * ur], axis=1).astype(jnp.bfloat16)
    w_t = jnp.stack([cos_t * ur + sin_t * ui, cos_t * ui - sin_t * ur], axis=1).astype(jnp.bfloat16)
    y_all = jnp.stack([v_real, v_imag], axis=0).astype(jnp.bfloat16)
    taps = z_t.shape[0]
    col_share = channels // freq_devices
    row_share = channels // data_devices
    y_cols = y_all.reshape(2, image_rows, bins_local, freq_devices, col_share)
    w_cols = w_t.reshape(taps, 2, image_rows, bins_local, freq_devices, col_share)
    first = jnp.einsum("teibr,eibfc->ftrc", z_t, y_cols, preferred_element_type=f32)
    second = jnp.einsum("eibr,teibfc->ftrc", y_all, w_cols, preferred_element_type=f32)
    gram_scale = 1.0 / math.sqrt(data_devices * freq_devices * slot_count)
    tap_scale = 2.0 * gram_scale / math.sqrt(total_bins)
    col_pieces = ((second - first) * tap_scale).astype(jnp.bfloat16)
    col_pieces = lax.all_to_all(col_pieces, "freq", split_axis=0, concat_axis=0, tiled=True)
    col_sum = jnp.sum(col_pieces.astype(f32), axis=0)
    z_devices = lax.axis_size("z")
    core_devices = lax.axis_size("c")
    row_pieces = jnp.transpose(
        col_sum.astype(jnp.bfloat16).reshape(taps, z_devices, core_devices, row_share, col_share),
        (2, 1, 0, 3, 4),
    )
    row_pieces = lax.all_to_all(row_pieces, "c", split_axis=0, concat_axis=0, tiled=True)
    row_pieces = jnp.sum(row_pieces.astype(f32), axis=0).astype(jnp.bfloat16)
    row_pieces = lax.all_to_all(row_pieces, "z", split_axis=0, concat_axis=0, tiled=True)
    tap_grad = jnp.sum(row_pieces.astype(f32), axis=0)
    return (returned, tap_grad)


def solution(mesh):
    cores = 2
    chips = Mesh(
        mesh.devices.reshape(mesh.shape["dp"] // cores, cores, mesh.shape["freq"]),
        ("z", "c", "freq"),
    )
    return jax.shard_map(
        local,
        mesh=chips,
        in_specs=(
            P(("z", "c", "freq"), None, None),
            P(("z", "c", "freq"), None, None),
            P(("z", "c", "freq")),
            P(),
            P("freq", None, None, None),
        ),
        out_specs=(P(("z", "c", "freq"), None, None), P(None, ("z", "c"), "freq")),
        check_vma=False,
    )
```
